256 devices in a mesh: pair: 64 (over y, x_hi, z), aux: 4 (over x_lo, core).
Axes of the slice: x: 4 (x_hi: 2, x_lo: 2; x = x_hi * 2 + x_lo), y: 4, z: 8, core: 2. Of those that a mesh axis runs over, the one named last changes fastest.
Arguments:
- amplitudes: bfloat16 [128, 16384], P('pair'), may hold values from -0.059814453 to 0.059814453
- factor_ca: bfloat16 [6400, 16384], P(('pair', 'aux')), may hold values from -0.5 to 0.5
- factor_db: bfloat16 [6400, 16384], P(('pair', 'aux')), may hold values from -0.5 to 0.5
Outputs:
- ladder: bfloat16 [128, 16384], P('pair', 'aux')
The draws below stay inside these ranges and needn't reach their ends.
All inputs are finite; a program needn't handle non-finite values.
Results may differ from the reference program's by a relative error of at most 0.02.
Values may be sent and summed in bfloat16 or wider, within the bound.
No kernel may reach another device: no remote copies, remote signals or barrier semaphores. Data moves between devices by JAX's collectives and lax.ppermute only.
A program may use at most 128 MiB of HBM per device.

```python
import jax
import jax.numpy as jnp
from jax import lax

NAUX = 6400
A = 128
B = 128
C = 128
D = 128
NIJ = 128
N_AUX = 4


def levels(key, dims, split, least, largest):
    def one(dim, shards_of):
        steps = jax.random.uniform(jax.random.fold_in(jax.random.fold_in(key, 6), dim), (shards_of,), jnp.float32, least / len(split), largest / len(split))
        return jnp.repeat(jnp.exp(steps), dims[dim] // shards_of).reshape((-1,) + (1,) * (len(dims) - dim - 1))

    gain = one(*split[0])
    for cut in split[1:]:
        gain = gain * one(*cut)
    return gain


def bell_draw(own_key, shape, scale, most, cuts=(), held_as=jnp.bfloat16):
    entries = scale * jax.random.normal(own_key, shape, jnp.float32)
    if cuts:
        entries = entries * levels(own_key, shape, cuts, -0.22, 0.18)
    return jnp.clip(entries, -most, most).astype(held_as)


def setup_inputs(seed: int = 0) -> dict:
    key_of = jax.random.split(jax.random.key(seed), 4)
    amplitudes = bell_draw(key_of[0], (NIJ, C * D), 0.01, 0.059814453, ((0, 64),))
    factor_ca = bell_draw(key_of[1], (NAUX, C * A), 160 ** -0.5, 0.5, ((0, 256),))
    factor_db = bell_draw(key_of[2], (NAUX, D * B), 160 ** -0.5, 0.5, ((0, 256),))
    return dict(amplitudes=amplitudes, factor_ca=factor_ca, factor_db=factor_db)


def reference(amplitudes, factor_ca, factor_db):
    right_flat = factor_db
    amps_flat = amplitudes
    left_cube = factor_ca.reshape(NAUX, C, A)
    quarter = NAUX // N_AUX

    def per_column(panel_col):
        total = jnp.zeros((C, D * B), jnp.float32)
        for block in range(N_AUX):
            left_rows = panel_col[block * quarter:(block + 1) * quarter]
            right_rows = right_flat[block * quarter:(block + 1) * quarter]
            partial_ints = jnp.dot(left_rows.T, right_rows, preferred_element_type=jnp.float32)
            rounded = lax.optimization_barrier(partial_ints.astype(jnp.bfloat16))
            total = total + rounded.astype(jnp.float32)
        ints_a = total.astype(jnp.bfloat16).reshape(C * D, B)
        return jnp.dot(amps_flat, ints_a, preferred_element_type=jnp.float32)

    stacked = lax.map(per_column, jnp.moveaxis(left_cube, 2, 0))
    return jnp.transpose(stacked, (1, 0, 2)).reshape(NIJ, A * B).astype(jnp.bfloat16)
```

```python
import functools

import jax
import jax.numpy as jnp
from jax import lax
from jax.experimental import pallas as pl
from jax.experimental.pallas import tpu as pltpu
from jax.sharding import PartitionSpec as P

A = 128
B = 128
C = 128
D = 128
I_BLOCK = 8
P_GROUP = 5


def ladder_kernel(n_p, n_aux, rpp, t_ref, r_ref, l_ref, out_ref, w_ref):
    t_blk = t_ref[...]
    for p0 in range(0, n_p, P_GROUP):
        pn = min(P_GROUP, n_p - p0)
        v = jnp.dot(
            t_blk, r_ref[:, p0 * B:(p0 + pn) * B], preferred_element_type=jnp.float32
        ).astype(jnp.bfloat16)
        for dp in range(pn):
            p = p0 + dp
            for i in range(I_BLOCK):
                w_ref[p * C:(p + 1) * C, i * B:(i + 1) * B] = v[i * C:(i + 1) * C, dp * B:(dp + 1) * B]
    y = jnp.dot(l_ref[...], w_ref[...], preferred_element_type=jnp.float32)
    apa = A // n_aux
    for i in range(I_BLOCK):
        for q in range(n_aux):
            out_ref[q, i // rpp, i % rpp] = y[q * apa:(q + 1) * apa, i * B:(i + 1) * B]


def local_ladder(t_all, factor_ca, factor_db, n_pair, n_aux):
    n_p = factor_ca.shape[0]
    nij = t_all.shape[0]
    rpp = nij // n_pair
    apa = A // n_aux
    t2 = t_all.reshape(nij * C, D)
    r2 = factor_db.reshape(n_p, D, B).transpose(1, 0, 2).reshape(D, n_p * B)
    l2 = factor_ca.reshape(n_p, C, A).transpose(2, 0, 1).reshape(A, n_p * C)
    steps = nij // I_BLOCK
    pb = I_BLOCK // rpp
    flops = 4 * nij * C * D * n_p * B
    kernel = functools.partial(ladder_kernel, n_p, n_aux, rpp)
    return pl.pallas_call(
        kernel,
        grid=(steps,),
        in_specs=[
            pl.BlockSpec((I_BLOCK * C, D), lambda g: (g, 0)),
            pl.BlockSpec((D, n_p * B), lambda g: (0, 0)),
            pl.BlockSpec((A, n_p * C), lambda g: (0, 0)),
        ],
        out_specs=pl.BlockSpec((n_aux, pb, rpp, apa, B), lambda g: (0, g, 0, 0, 0)),
        out_shape=jax.ShapeDtypeStruct((n_aux, n_pair, rpp, apa, B), jnp.float32),
        scratch_shapes=[pltpu.VMEM((n_p * C, I_BLOCK * B), jnp.bfloat16)],
        compiler_params=pltpu.CompilerParams(vmem_limit_bytes=48 * 1024 * 1024),
        cost_estimate=pl.CostEstimate(
            flops=flops, transcendentals=0,
            bytes_accessed=2 * (t2.size + r2.size + l2.size) + 4 * nij * A * B,
        ),
    )(t2, r2, l2)


def local(amplitudes, factor_ca, factor_db):
    n_pair = lax.axis_size("pair")
    n_aux = lax.axis_size("aux")
    t_all = lax.all_gather(amplitudes, "pair", axis=0, tiled=True)
    y = local_ladder(t_all, factor_ca, factor_db, n_pair, n_aux)
    rpp = y.shape[2]
    y = y.reshape(n_aux, n_pair, -1)
    y = lax.psum_scatter(y, "aux", scatter_dimension=0, tiled=True)
    mine = lax.psum_scatter(y[0], "pair", scatter_dimension=0, tiled=True)
    return mine.reshape(rpp, -1).astype(jnp.bfloat16)


def solution(mesh):
    return jax.shard_map(
        local,
        mesh=mesh,
        in_specs=(P("pair", None), P(("pair", "aux"), None), P(("pair", "aux"), None)),
        out_specs=P("pair", "aux"),
        check_vma=False,
    )
```

```python
import functools

import jax
import jax.numpy as jnp
from jax import lax
from jax.experimental import pallas as pl
from jax.experimental.pallas import tpu as pltpu
from jax.sharding import PartitionSpec as P

A = 128
B = 128
C = 128
D = 128
I_BLOCK = 8
P_GROUP = 5


def ladder_kernel(n_p, n_aux, rpp, t_ref, r_ref, l_ref, out_ref, w_ref):
    t_blk = t_ref[...]
    for p0 in range(0, n_p, P_GROUP):
        pn = min(P_GROUP, n_p - p0)
        v = jnp.dot(
            t_blk, r_ref[:, p0 * B:(p0 + pn) * B], preferred_element_type=jnp.float32
        ).astype(jnp.bfloat16)
        for dp in range(pn):
            p = p0 + dp
            for i in range(I_BLOCK):
                w_ref[p * C:(p + 1) * C, i * B:(i + 1) * B] = v[i * C:(i + 1) * C, dp * B:(dp + 1) * B]
    y = jnp.dot(l_ref[...], w_ref[...], preferred_element_type=jnp.float32)
    apa = A // n_aux
    for i in range(I_BLOCK):
        for q in range(n_aux):
            out_ref[q, i // rpp, i % rpp] = y[q * apa:(q + 1) * apa, i * B:(i + 1) * B]


def local_ladder(t_all, factor_ca, factor_db, n_pair, n_aux):
    n_p = factor_ca.shape[0]
    nij = t_all.shape[0]
    rpp = nij // n_pair
    apa = A // n_aux
    t2 = t_all.reshape(nij * C, D)
    r2 = factor_db.reshape(n_p, D, B).transpose(1, 0, 2).reshape(D, n_p * B)
    l2 = factor_ca.reshape(n_p, C, A).transpose(2, 0, 1).reshape(A, n_p * C)
    steps = nij // I_BLOCK
    pb = I_BLOCK // rpp
    flops = 4 * nij * C * D * n_p * B
    kernel = functools.partial(ladder_kernel, n_p, n_aux, rpp)
    return pl.pallas_call(
        kernel,
        grid=(steps,),
        in_specs=[
            pl.BlockSpec((I_BLOCK * C, D), lambda g: (g, 0)),
            pl.BlockSpec((D, n_p * B), lambda g: (0, 0)),
            pl.BlockSpec((A, n_p * C), lambda g: (0, 0)),
        ],
        out_specs=pl.BlockSpec((n_aux, pb, rpp, apa, B), lambda g: (0, g, 0, 0, 0)),
        out_shape=jax.ShapeDtypeStruct((n_aux, n_pair, rpp, apa, B), jnp.float32),
        scratch_shapes=[pltpu.VMEM((n_p * C, I_BLOCK * B), jnp.bfloat16)],
        compiler_params=pltpu.CompilerParams(vmem_limit_bytes=48 * 1024 * 1024),
        cost_estimate=pl.CostEstimate(
            flops=flops, transcendentals=0,
            bytes_accessed=2 * (t2.size + r2.size + l2.size) + 4 * nij * A * B,
        ),
    )(t2, r2, l2)


def local(amplitudes, factor_ca, factor_db):
    n_pair = lax.axis_size("pair")
    n_aux = lax.axis_size("aux")
    t_all = lax.all_gather(amplitudes, "pair", axis=0, tiled=True)
    y = local_ladder(t_all, factor_ca, factor_db, n_pair, n_aux)
    rpp = y.shape[2]
    y = y.reshape(n_aux, n_pair, -1)
    y = lax.psum_scatter(y, "aux", scatter_dimension=0, tiled=True)
    parts = lax.all_to_all(y[0], "pair", split_axis=0, concat_axis=0, tiled=True)
    mine = jnp.sum(parts, axis=0)
    return mine.reshape(rpp, -1).astype(jnp.bfloat16)


def solution(mesh):
    return jax.shard_map(
        local,
        mesh=mesh,
        in_specs=(P("pair", None), P(("pair", "aux"), None), P(("pair", "aux"), None)),
        out_specs=P("pair", "aux"),
        check_vma=False,
    )
```

```python
import functools

import jax
import jax.numpy as jnp
from jax import lax
from jax.experimental import pallas as pl
from jax.experimental.pallas import tpu as pltpu
from jax.sharding import PartitionSpec as P

A = 128
B = 128
C = 128
D = 128
I_BLOCK = 8
P_GROUP = 5


def ladder_kernel(n_p, n_aux, rpp, t_ref, r_ref, l_ref, out_ref, w_ref):
    cq = C // n_aux
    t_blk = t_ref[...].reshape(n_aux * I_BLOCK * cq, D)
    for p0 in range(0, n_p, P_GROUP):
        pn = min(P_GROUP, n_p - p0)
        v = jnp.dot(
            t_blk, r_ref[:, p0 * B:(p0 + pn) * B], preferred_element_type=jnp.float32
        ).astype(jnp.bfloat16)
        for dp in range(pn):
            p = p0 + dp
            for q in range(n_aux):
                for i in range(I_BLOCK):
                    r0 = (q * I_BLOCK + i) * cq
                    w_ref[p * C + q * cq:p * C + (q + 1) * cq, i * B:(i + 1) * B] = (
                        v[r0:r0 + cq, dp * B:(dp + 1) * B])
    y = jnp.dot(l_ref[...], w_ref[...], preferred_element_type=jnp.float32)
    apa = A // n_aux
    for i in range(I_BLOCK):
        for q in range(n_aux):
            out_ref[q, i // rpp, i % rpp] = y[q * apa:(q + 1) * apa, i * B:(i + 1) * B]


def local_ladder(t_all, factor_ca, factor_db, n_pair, n_aux):
    n_p = factor_ca.shape[0]
    nij = t_all.shape[1]
    rpp = nij // n_pair
    apa = A // n_aux
    t2 = t_all
    r2 = factor_db.reshape(n_p, D, B).transpose(1, 0, 2).reshape(D, n_p * B)
    l2 = factor_ca.reshape(n_p, C, A).transpose(2, 0, 1).reshape(A, n_p * C)
    steps = nij // I_BLOCK
    pb = I_BLOCK // rpp
    flops = 4 * nij * C * D * n_p * B
    kernel = functools.partial(ladder_kernel, n_p, n_aux, rpp)
    return pl.pallas_call(
        kernel,
        grid=(steps,),
        in_specs=[
            pl.BlockSpec((n_aux, I_BLOCK, C // n_aux, D), lambda g: (0, g, 0, 0)),
            pl.BlockSpec((D, n_p * B), lambda g: (0, 0)),
            pl.BlockSpec((A, n_p * C), lambda g: (0, 0)),
        ],
        out_specs=pl.BlockSpec((n_aux, pb, rpp, apa, B), lambda g: (0, g, 0, 0, 0)),
        out_shape=jax.ShapeDtypeStruct((n_aux, n_pair, rpp, apa, B), jnp.float32),
        scratch_shapes=[pltpu.VMEM((n_p * C, I_BLOCK * B), jnp.bfloat16)],
        compiler_params=pltpu.CompilerParams(vmem_limit_bytes=48 * 1024 * 1024),
        cost_estimate=pl.CostEstimate(
            flops=flops, transcendentals=0,
            bytes_accessed=2 * (t2.size + r2.size + l2.size) + 4 * nij * A * B,
        ),
    )(t2, r2, l2)


def local(amplitudes, factor_ca, factor_db):
    n_pair = lax.axis_size("pair")
    n_aux = lax.axis_size("aux")
    cq = C // n_aux
    q = lax.axis_index("aux")
    amps_q = lax.dynamic_slice_in_dim(amplitudes, q * cq * D, cq * D, axis=1)
    amps_q = amps_q.reshape(amplitudes.shape[0], cq, D)
    t_q = lax.all_gather(amps_q, "pair", axis=0, tiled=True)
    t_all = lax.all_gather(t_q, "aux", axis=0)
    y = local_ladder(t_all, factor_ca, factor_db, n_pair, n_aux)
    rpp = y.shape[2]
    y = y.reshape(n_aux, n_pair, rpp * y.shape[3], B)
    y = lax.psum_scatter(y, "aux", scatter_dimension=0, tiled=True)
    parts = lax.all_to_all(y[0], "pair", split_axis=0, concat_axis=0, tiled=True)
    mine = jnp.sum(parts, axis=0).astype(jnp.bfloat16)
    return mine.reshape(rpp, -1)


def solution(mesh):
    return jax.shard_map(
        local,
        mesh=mesh,
        in_specs=(P("pair", None), P(("pair", "aux"), None), P(("pair", "aux"), None)),
        out_specs=P("pair", "aux"),
        check_vma=False,
    )
```

```python
import functools

import jax
import jax.numpy as jnp
from jax import lax
from jax.experimental import pallas as pl
from jax.experimental.pallas import tpu as pltpu
from jax.sharding import PartitionSpec as P

A = 128
B = 128
C = 128
D = 128
I_BLOCK = 8
P_GROUP = 5


def ladder_kernel(n_p, n_aux, rpp, t_ref, r_ref, l_ref, out_ref, w_ref):
    t_blk = t_ref[...]
    for p0 in range(0, n_p, P_GROUP):
        pn = min(P_GROUP, n_p - p0)
        v = jnp.dot(
            t_blk, r_ref[:, p0 * B:(p0 + pn) * B], preferred_element_type=jnp.float32
        ).astype(jnp.bfloat16)
        for dp in range(pn):
            p = p0 + dp
            for i in range(I_BLOCK):
                w_ref[p * C:(p + 1) * C, i * B:(i + 1) * B] = v[i * C:(i + 1) * C, dp * B:(dp + 1) * B]
    y = jnp.dot(l_ref[...], w_ref[...], preferred_element_type=jnp.float32)
    apa = A // n_aux
    for i in range(I_BLOCK):
        for q in range(n_aux):
            out_ref[q, i // rpp, i % rpp] = y[q * apa:(q + 1) * apa, i * B:(i + 1) * B]


def local_ladder(t_all, factor_ca, factor_db, n_pair, n_aux):
    n_p = factor_ca.shape[0]
    nij = t_all.shape[0]
    rpp = nij // n_pair
    apa = A // n_aux
    t2 = t_all.reshape(nij * C, D)
    r2 = factor_db.reshape(n_p, D, B).transpose(1, 0, 2).reshape(D, n_p * B)
    l2 = factor_ca.reshape(n_p, C, A).transpose(2, 0, 1).reshape(A, n_p * C)
    steps = nij // I_BLOCK
    pb = I_BLOCK // rpp
    flops = 4 * nij * C * D * n_p * B
    kernel = functools.partial(ladder_kernel, n_p, n_aux, rpp)
    return pl.pallas_call(
        kernel,
        grid=(steps,),
        in_specs=[
            pl.BlockSpec((I_BLOCK * C, D), lambda g: (g, 0)),
            pl.BlockSpec((D, n_p * B), lambda g: (0, 0)),
            pl.BlockSpec((A, n_p * C), lambda g: (0, 0)),
        ],
        out_specs=pl.BlockSpec((n_aux, pb, rpp, apa, B), lambda g: (0, g, 0, 0, 0)),
        out_shape=jax.ShapeDtypeStruct((n_aux, n_pair, rpp, apa, B), jnp.float32),
        scratch_shapes=[pltpu.VMEM((n_p * C, I_BLOCK * B), jnp.bfloat16)],
        compiler_params=pltpu.CompilerParams(vmem_limit_bytes=48 * 1024 * 1024),
        cost_estimate=pl.CostEstimate(
            flops=flops, transcendentals=0,
            bytes_accessed=2 * (t2.size + r2.size + l2.size) + 4 * nij * A * B,
        ),
    )(t2, r2, l2)


def bit_order(n_bits, far_first):
    if n_bits == 6:
        order = [2, 5, 3, 1, 4, 0]
    else:
        order = list(range(n_bits - 1, -1, -1))
    return order if far_first else order[::-1]


def xor_perm(n, b):
    return [(i, i ^ (1 << b)) for i in range(n)]


def gather_pair(x, n):
    n_bits = n.bit_length() - 1
    me = lax.axis_index("pair")
    order = bit_order(n_bits, True)
    buf = x
    for k, b in enumerate(order):
        recv = lax.ppermute(buf, "pair", xor_perm(n, b))
        low = ((me >> b) & 1) == 0
        lo = jnp.where(low, buf, recv)
        hi = jnp.where(low, recv, buf)
        buf = jnp.stack([lo, hi], axis=k)
    axes = [order.index(b) for b in range(n_bits - 1, -1, -1)]
    buf = buf.transpose(axes + list(range(n_bits, buf.ndim)))
    return buf.reshape((n,) + x.shape)


def reduce_pair(y, n):
    n_bits = n.bit_length() - 1
    me = lax.axis_index("pair")
    blk = y.shape[1:]
    buf = y.reshape((2,) * n_bits + blk)
    axes = list(range(n_bits - 1, -1, -1))
    for b in bit_order(n_bits, False):
        ax = axes.index(b)
        mine = (me >> b) & 1
        keep = lax.dynamic_index_in_dim(buf, mine, axis=ax, keepdims=False)
        send = lax.dynamic_index_in_dim(buf, 1 - mine, axis=ax, keepdims=False)
        recv = lax.ppermute(send.astype(jnp.bfloat16), "pair", xor_perm(n, b))
        buf = keep + recv.astype(jnp.float32)
        axes.pop(ax)
    return buf


def local(amplitudes, factor_ca, factor_db):
    n_pair = lax.axis_size("pair")
    n_aux = lax.axis_size("aux")
    rows = amplitudes.shape[0]
    t_all = gather_pair(amplitudes.reshape(rows * C, D), n_pair).reshape(n_pair * rows, C * D)
    y = local_ladder(t_all, factor_ca, factor_db, n_pair, n_aux)
    rpp = y.shape[2]
    y = y.reshape(n_aux, n_pair, rpp * y.shape[3], B).astype(jnp.bfloat16)
    y = lax.psum_scatter(y, "aux", scatter_dimension=0, tiled=True)
    mine = reduce_pair(y[0].astype(jnp.float32), n_pair).astype(jnp.bfloat16)
    return mine.reshape(rpp, -1)


def solution(mesh):
    return jax.shard_map(
        local,
        mesh=mesh,
        in_specs=(P("pair", None), P(("pair", "aux"), None), P(("pair", "aux"), None)),
        out_specs=P("pair", "aux"),
        check_vma=False,
    )
```

```python
import functools

import jax
import jax.numpy as jnp
from jax import lax
from jax.experimental import pallas as pl
from jax.experimental.pallas import tpu as pltpu
from jax.sharding import PartitionSpec as P

A = 128
B = 128
C = 128
D = 128
I_BLOCK = 8
P_GROUP = 5
SMALL_SEND = 131072


def ladder_kernel(n_p, n_aux, rpp, t_ref, r_ref, l_ref, out_ref, w_ref):
    cq = C // n_aux
    t_blk = t_ref[...].reshape(n_aux * I_BLOCK * cq, D)
    for p0 in range(0, n_p, P_GROUP):
        pn = min(P_GROUP, n_p - p0)
        v = jnp.dot(
            t_blk, r_ref[:, p0 * B:(p0 + pn) * B], preferred_element_type=jnp.float32
        ).astype(jnp.bfloat16)
        for dp in range(pn):
            p = p0 + dp
            for q in range(n_aux):
                for i in range(I_BLOCK):
                    r0 = (q * I_BLOCK + i) * cq
                    w_ref[p * C + q * cq:p * C + (q + 1) * cq, i * B:(i + 1) * B] = (
                        v[r0:r0 + cq, dp * B:(dp + 1) * B])
    y = jnp.dot(l_ref[...], w_ref[...], preferred_element_type=jnp.float32)
    apa = A // n_aux
    for i in range(I_BLOCK):
        for q in range(n_aux):
            out_ref[q, i // rpp, i % rpp] = y[q * apa:(q + 1) * apa, i * B:(i + 1) * B].astype(out_ref.dtype)


def local_ladder(t_all, factor_ca, factor_db, n_pair, n_aux):
    n_p = factor_ca.shape[0]
    nij = t_all.shape[1]
    rpp = nij // n_pair
    apa = A // n_aux
    t2 = t_all
    r2 = factor_db.reshape(n_p, D, B).transpose(1, 0, 2).reshape(D, n_p * B)
    l2 = factor_ca.reshape(n_p, C, A).transpose(2, 0, 1).reshape(A, n_p * C)
    steps = nij // I_BLOCK
    pb = I_BLOCK // rpp
    flops = 4 * nij * C * D * n_p * B
    kernel = functools.partial(ladder_kernel, n_p, n_aux, rpp)
    return pl.pallas_call(
        kernel,
        grid=(steps,),
        in_specs=[
            pl.BlockSpec((n_aux, I_BLOCK, C // n_aux, D), lambda g: (0, g, 0, 0)),
            pl.BlockSpec((D, n_p * B), lambda g: (0, 0)),
            pl.BlockSpec((A, n_p * C), lambda g: (0, 0)),
        ],
        out_specs=pl.BlockSpec((n_aux, pb, rpp, apa, B), lambda g: (0, g, 0, 0, 0)),
        out_shape=jax.ShapeDtypeStruct((n_aux, n_pair, rpp, apa, B), jnp.bfloat16),
        scratch_shapes=[pltpu.VMEM((n_p * C, I_BLOCK * B), jnp.bfloat16)],
        compiler_params=pltpu.CompilerParams(vmem_limit_bytes=48 * 1024 * 1024),
        cost_estimate=pl.CostEstimate(
            flops=flops, transcendentals=0,
            bytes_accessed=2 * (t2.size + r2.size + l2.size) + 2 * nij * A * B,
        ),
    )(t2, r2, l2)


def bit_order(axis, n_bits, far_first):
    if axis == "pair" and n_bits == 6:
        order = [2, 5, 3, 1, 4, 0]
    else:
        order = list(range(n_bits - 1, -1, -1))
    return order if far_first else order[::-1]


def xor_perm(n, b):
    return [(i, i ^ (1 << b)) for i in range(n)]


def gather_axis(x, axis, n):
    n_bits = n.bit_length() - 1
    me = lax.axis_index(axis)
    order = bit_order(axis, n_bits, True)
    buf = x
    for k, b in enumerate(order):
        recv = lax.ppermute(buf, axis, xor_perm(n, b))
        low = ((me >> b) & 1) == 0
        lo = jnp.where(low, buf, recv)
        hi = jnp.where(low, recv, buf)
        buf = jnp.stack([lo, hi], axis=k)
    axes = [order.index(b) for b in range(n_bits - 1, -1, -1)]
    buf = buf.transpose(axes + list(range(n_bits, buf.ndim)))
    return buf.reshape((n,) + x.shape)


def reduce_axis(y, axis, n):
    n_bits = n.bit_length() - 1
    me = lax.axis_index(axis)
    blk = y.shape[1:]
    buf = y.reshape((2,) * n_bits + blk)
    axes = list(range(n_bits - 1, -1, -1))
    for b in bit_order(axis, n_bits, False):
        ax = axes.index(b)
        mine = (me >> b) & 1
        keep = lax.dynamic_index_in_dim(buf, mine, axis=ax, keepdims=False)
        send = lax.dynamic_index_in_dim(buf, 1 - mine, axis=ax, keepdims=False)
        wire = jnp.bfloat16 if send.size > SMALL_SEND else jnp.float32
        recv = lax.ppermute(send.astype(wire), axis, xor_perm(n, b))
        buf = keep.astype(jnp.float32) + recv.astype(jnp.float32)
        axes.pop(ax)
    return buf


def local(amplitudes, factor_ca, factor_db):
    n_pair = lax.axis_size("pair")
    n_aux = lax.axis_size("aux")
    rows = amplitudes.shape[0]
    cq = C // n_aux
    q = lax.axis_index("aux")
    amps_q = lax.dynamic_slice_in_dim(amplitudes, q * cq * D, cq * D, axis=1)
    amps_q = amps_q.reshape(rows * cq, D)
    t_q = gather_axis(amps_q, "pair", n_pair).reshape(n_pair * rows, cq, D)
    t_all = gather_axis(t_q, "aux", n_aux)
    y = local_ladder(t_all, factor_ca, factor_db, n_pair, n_aux)
    rpp = y.shape[2]
    y = y.reshape(n_aux, n_pair, rpp * y.shape[3], B)
    y = reduce_axis(y, "aux", n_aux)
    mine = reduce_axis(y, "pair", n_pair).astype(jnp.bfloat16)
    return mine.reshape(rpp, -1)


def solution(mesh):
    return jax.shard_map(
        local,
        mesh=mesh,
        in_specs=(P("pair", None), P(("pair", "aux"), None), P(("pair", "aux"), None)),
        out_specs=P("pair", "aux"),
        check_vma=False,
    )
```

```python
import functools

import jax
import jax.numpy as jnp
from jax import lax
from jax.experimental import pallas as pl
from jax.experimental.pallas import tpu as pltpu
from jax.sharding import PartitionSpec as P

A = 128
B = 128
C = 128
D = 128
I_BLOCK = 8
P_GROUP = 5
SMALL_SEND = 65536


def ladder_kernel(n_p, n_aux, rpp, t_ref, r_ref, l_ref, out_ref, w_ref):
    cq = C // n_aux
    t_blk = t_ref[...].reshape(n_aux * I_BLOCK * cq, D)
    for p0 in range(0, n_p, P_GROUP):
        pn = min(P_GROUP, n_p - p0)
        v = jnp.dot(
            t_blk, r_ref[:, p0 * B:(p0 + pn) * B], preferred_element_type=jnp.float32
        ).astype(jnp.bfloat16)
        for dp in range(pn):
            p = p0 + dp
            for q in range(n_aux):
                for i in range(I_BLOCK):
                    r0 = (q * I_BLOCK + i) * cq
                    w_ref[p * C + q * cq:p * C + (q + 1) * cq, i * B:(i + 1) * B] = (
                        v[r0:r0 + cq, dp * B:(dp + 1) * B])
    y = jnp.dot(l_ref[...], w_ref[...], preferred_element_type=jnp.float32)
    apa = A // n_aux
    for i in range(I_BLOCK):
        for q in range(n_aux):
            out_ref[i // rpp, q, i % rpp] = y[q * apa:(q + 1) * apa, i * B:(i + 1) * B].astype(out_ref.dtype)


def local_ladder(t_all, factor_ca, factor_db, n_pair, n_aux):
    n_p = factor_ca.shape[0]
    nij = t_all.shape[1]
    rpp = nij // n_pair
    apa = A // n_aux
    t2 = t_all
    r2 = factor_db.reshape(n_p, D, B).transpose(1, 0, 2).reshape(D, n_p * B)
    l2 = factor_ca.reshape(n_p, C, A).transpose(2, 0, 1).reshape(A, n_p * C)
    steps = nij // I_BLOCK
    pb = I_BLOCK // rpp
    flops = 4 * nij * C * D * n_p * B
    kernel = functools.partial(ladder_kernel, n_p, n_aux, rpp)
    return pl.pallas_call(
        kernel,
        grid=(steps,),
        in_specs=[
            pl.BlockSpec((n_aux, I_BLOCK, C // n_aux, D), lambda g: (0, g, 0, 0)),
            pl.BlockSpec((D, n_p * B), lambda g: (0, 0)),
            pl.BlockSpec((A, n_p * C), lambda g: (0, 0)),
        ],
        out_specs=pl.BlockSpec((pb, n_aux, rpp, apa, B), lambda g: (g, 0, 0, 0, 0)),
        out_shape=jax.ShapeDtypeStruct((n_pair, n_aux, rpp, apa, B), jnp.bfloat16),
        scratch_shapes=[pltpu.VMEM((n_p * C, I_BLOCK * B), jnp.bfloat16)],
        compiler_params=pltpu.CompilerParams(vmem_limit_bytes=48 * 1024 * 1024),
        cost_estimate=pl.CostEstimate(
            flops=flops, transcendentals=0,
            bytes_accessed=2 * (t2.size + r2.size + l2.size) + 2 * nij * A * B,
        ),
    )(t2, r2, l2)


def two_orders(n_pair, n_aux):
    if (n_pair, n_aux) == (64, 4):
        return [0, 1, 2, 6, 3, 5, 7, 4], [0, 2, 1, 3, 6, 7, 5, 4]
    n_bits = (n_pair * n_aux).bit_length() - 1
    first = list(range(n_bits))
    return first, first[1:] + first[:1]


def xor_perm(n, b):
    return [(i, i ^ (1 << b)) for i in range(n)]


def gather_bits(x, axes, n, order, target):
    n_bits = n.bit_length() - 1
    me = lax.axis_index(axes)
    buf = x
    for k, b in enumerate(order):
        recv = lax.ppermute(buf, axes, xor_perm(n, b))
        low = ((me >> b) & 1) == 0
        lo = jnp.where(low, buf, recv)
        hi = jnp.where(low, recv, buf)
        buf = jnp.stack([lo, hi], axis=k)
    perm = [order.index(b) for b in target]
    return buf.transpose(perm + list(range(n_bits, buf.ndim)))


def reduce_bits(y, axes, n, order):
    n_bits = n.bit_length() - 1
    me = lax.axis_index(axes)
    blk = y.shape[1:]
    buf = y.reshape((2,) * n_bits + blk)
    live = list(range(n_bits - 1, -1, -1))
    for b in order:
        ax = live.index(b)
        mine = (me >> b) & 1
        keep = lax.dynamic_index_in_dim(buf, mine, axis=ax, keepdims=False)
        send = lax.dynamic_index_in_dim(buf, 1 - mine, axis=ax, keepdims=False)
        wire = jnp.bfloat16 if send.size > SMALL_SEND else jnp.float32
        recv = lax.ppermute(send.astype(wire), axes, xor_perm(n, b))
        buf = keep.astype(jnp.float32) + recv.astype(jnp.float32)
        live.pop(ax)
    return buf


def local(amplitudes, factor_ca, factor_db):
    n_pair = lax.axis_size("pair")
    n_aux = lax.axis_size("aux")
    n = n_pair * n_aux
    both = ("pair", "aux")
    order_a, order_b = two_orders(n_pair, n_aux)
    rows = amplitudes.shape[0]
    cq = C // n_aux
    q = lax.axis_index("aux")
    amps_q = lax.dynamic_slice_in_dim(amplitudes, q * cq * D, cq * D, axis=1)
    amps_q = amps_q.reshape(rows, cq, D)
    half = cq // 2
    n_bits = n.bit_length() - 1
    aux_bits = n_aux.bit_length() - 1
    target = list(range(aux_bits - 1, -1, -1)) + list(range(n_bits - 1, aux_bits - 1, -1))
    t_halves = [
        gather_bits(amps_q[:, h * half:(h + 1) * half], both, n, order[::-1], target)
        .reshape(n_aux, n_pair * rows, half, D)
        for h, order in enumerate((order_a, order_b))
    ]
    t_all = jnp.concatenate(t_halves, axis=2)
    y = local_ladder(t_all, factor_ca, factor_db, n_pair, n_aux)
    rpp = y.shape[2]
    y = y.reshape(n, rpp * y.shape[3], B)
    split = y.shape[1] // 2
    mine = jnp.concatenate([
        reduce_bits(y[:, h * split:(h + 1) * split], both, n, order)
        for h, order in enumerate((order_a, order_b))
    ], axis=0).astype(jnp.bfloat16)
    return mine.reshape(rpp, -1)


def solution(mesh):
    return jax.shard_map(
        local,
        mesh=mesh,
        in_specs=(P("pair", None), P(("pair", "aux"), None), P(("pair", "aux"), None)),
        out_specs=P("pair", "aux"),
        check_vma=False,
    )
```

```python
import functools

import jax
import jax.numpy as jnp
from jax import lax
from jax.experimental import pallas as pl
from jax.experimental.pallas import tpu as pltpu
from jax.sharding import PartitionSpec as P

A = 128
B = 128
C = 128
D = 128
I_BLOCK = 8
P_GROUP = 5
SMALL_SEND = 65536


def ladder_kernel(n_p, n_aux, rpp, t_ref, r_ref, l_ref, out_ref, w_ref):
    cq = C // n_aux
    t_blk = t_ref[...].reshape(n_aux * I_BLOCK * cq, D)
    for p0 in range(0, n_p, P_GROUP):
        pn = min(P_GROUP, n_p - p0)
        v = jnp.dot(
            t_blk, r_ref[:, p0 * B:(p0 + pn) * B], preferred_element_type=jnp.float32
        ).astype(jnp.bfloat16)
        for dp in range(pn):
            p = p0 + dp
            for q in range(n_aux):
                for i in range(I_BLOCK):
                    r0 = (q * I_BLOCK + i) * cq
                    w_ref[p * C + q * cq:p * C + (q + 1) * cq, i * B:(i + 1) * B] = (
                        v[r0:r0 + cq, dp * B:(dp + 1) * B])
    y = jnp.dot(l_ref[...], w_ref[...], preferred_element_type=jnp.float32)
    apa = A // n_aux
    for i in range(I_BLOCK):
        for q in range(n_aux):
            out_ref[i // rpp, q, i % rpp] = y[q * apa:(q + 1) * apa, i * B:(i + 1) * B].astype(out_ref.dtype)


def local_ladder(t_all, factor_ca, factor_db, n_pair, n_aux):
    n_p = factor_ca.shape[0]
    nij = t_all.shape[1]
    rpp = nij // n_pair
    apa = A // n_aux
    t2 = t_all
    r2 = factor_db.reshape(n_p, D, B).transpose(1, 0, 2).reshape(D, n_p * B)
    l2 = factor_ca.reshape(n_p, C, A).transpose(2, 0, 1).reshape(A, n_p * C)
    steps = nij // I_BLOCK
    pb = I_BLOCK // rpp
    flops = 4 * nij * C * D * n_p * B
    kernel = functools.partial(ladder_kernel, n_p, n_aux, rpp)
    return pl.pallas_call(
        kernel,
        grid=(steps,),
        in_specs=[
            pl.BlockSpec((n_aux, I_BLOCK, C // n_aux, D), lambda g: (0, g, 0, 0)),
            pl.BlockSpec((D, n_p * B), lambda g: (0, 0)),
            pl.BlockSpec((A, n_p * C), lambda g: (0, 0)),
        ],
        out_specs=pl.BlockSpec((pb, n_aux, rpp, apa, B), lambda g: (g, 0, 0, 0, 0)),
        out_shape=jax.ShapeDtypeStruct((n_pair, n_aux, rpp, apa, B), jnp.bfloat16),
        scratch_shapes=[pltpu.VMEM((n_p * C, I_BLOCK * B), jnp.bfloat16)],
        compiler_params=pltpu.CompilerParams(vmem_limit_bytes=48 * 1024 * 1024),
        cost_estimate=pl.CostEstimate(
            flops=flops, transcendentals=0,
            bytes_accessed=2 * (t2.size + r2.size + l2.size) + 2 * nij * A * B,
        ),
    )(t2, r2, l2)


def plan(n_pair, n_aux):
    if (n_pair, n_aux) == (64, 4):
        return [0], ([1, 2], [2, 1]), [6, 3, 5, 7, 4]
    n_bits = (n_pair * n_aux).bit_length() - 1
    rest = list(range(2, n_bits))
    return [0], ([1], [1]), rest


def xor_perm(n, b):
    return [(i, i ^ (1 << b)) for i in range(n)]


def gather_step(buf, axes, n, me, b, k):
    recv = lax.ppermute(buf, axes, xor_perm(n, b))
    low = ((me >> b) & 1) == 0
    lo = jnp.where(low, buf, recv)
    hi = jnp.where(low, recv, buf)
    return jnp.stack([lo, hi], axis=k)


def gather_bits(x, axes, n, first, pair_orders, last, target, split_axis):
    n_bits = n.bit_length() - 1
    me = lax.axis_index(axes)
    buf = x
    for k, b in enumerate(first):
        buf = gather_step(buf, axes, n, me, b, k)
    ax = len(first) + split_axis
    size = buf.shape[ax] // 2
    halves = []
    for h, tail in enumerate(pair_orders):
        part = lax.slice_in_dim(buf, h * size, (h + 1) * size, axis=ax)
        order = first + tail + last
        for k, b in enumerate(tail + last):
            part = gather_step(part, axes, n, me, b, len(first) + k)
        perm = [order.index(b) for b in target]
        halves.append(part.transpose(perm + list(range(n_bits, part.ndim))))
    return jnp.concatenate(halves, axis=n_bits + split_axis)


def reduce_step(buf, axes, n, me, live, b):
    ax = live.index(b)
    mine = (me >> b) & 1
    keep = lax.dynamic_index_in_dim(buf, mine, axis=ax, keepdims=False)
    send = lax.dynamic_index_in_dim(buf, 1 - mine, axis=ax, keepdims=False)
    wire = jnp.bfloat16 if send.size > SMALL_SEND else jnp.float32
    recv = lax.ppermute(send.astype(wire), axes, xor_perm(n, b))
    live.pop(ax)
    return keep.astype(jnp.float32) + recv.astype(jnp.float32)


def reduce_bits(y, axes, n, first, pair_orders, last):
    n_bits = n.bit_length() - 1
    me = lax.axis_index(axes)
    buf = y.reshape((2,) * n_bits + y.shape[1:])
    live = list(range(n_bits - 1, -1, -1))
    for b in first:
        buf = reduce_step(buf, axes, n, me, live, b)
    ax = len(live)
    size = buf.shape[ax] // 2
    halves = []
    for order in pair_orders:
        part = lax.slice_in_dim(buf, size * len(halves), size * (len(halves) + 1), axis=ax)
        part_live = list(live)
        for b in order:
            part = reduce_step(part, axes, n, me, part_live, b)
        halves.append(part)
    live = part_live
    buf = jnp.concatenate(halves, axis=len(live))
    for b in last:
        buf = reduce_step(buf, axes, n, me, live, b)
    return buf


def local(amplitudes, factor_ca, factor_db):
    n_pair = lax.axis_size("pair")
    n_aux = lax.axis_size("aux")
    n = n_pair * n_aux
    both = ("pair", "aux")
    first, pair_orders, last = plan(n_pair, n_aux)
    rows = amplitudes.shape[0]
    cq = C // n_aux
    q = lax.axis_index("aux")
    amps_q = lax.dynamic_slice_in_dim(amplitudes, q * cq * D, cq * D, axis=1)
    amps_q = amps_q.reshape(rows, cq, D)
    n_bits = n.bit_length() - 1
    aux_bits = n_aux.bit_length() - 1
    target = list(range(aux_bits - 1, -1, -1)) + list(range(n_bits - 1, aux_bits - 1, -1))
    t_all = gather_bits(amps_q, both, n, last[::-1], [o[::-1] for o in pair_orders], first[::-1], target, 1)
    t_all = t_all.reshape(n_aux, n_pair * rows, cq, D)
    y = local_ladder(t_all, factor_ca, factor_db, n_pair, n_aux)
    rpp = y.shape[2]
    y = y.reshape(n, rpp * y.shape[3], B)
    mine = reduce_bits(y, both, n, first, pair_orders, last).astype(jnp.bfloat16)
    return mine.reshape(rpp, -1)


def solution(mesh):
    return jax.shard_map(
        local,
        mesh=mesh,
        in_specs=(P("pair", None), P(("pair", "aux"), None), P(("pair", "aux"), None)),
        out_specs=P("pair", "aux"),
        check_vma=False,
    )
```

```python
import functools

import jax
import jax.numpy as jnp
from jax import lax
from jax.experimental import pallas as pl
from jax.experimental.pallas import tpu as pltpu
from jax.sharding import PartitionSpec as P

A = 128
B = 128
C = 128
D = 128
I_BLOCK = 8
P_GROUP = 5
SMALL_SEND = 65536


def ladder_kernel(n_p, n_aux, rpp, t_ref, fb_ref, fa_ref, out_ref, w_ref, r_ref, l_ref):
    @pl.when(pl.program_id(0) == 0)
    def _():
        for p in range(n_p):
            r_ref[:, p * B:(p + 1) * B] = fb_ref[p]
            l_ref[:, p * C:(p + 1) * C] = fa_ref[p].astype(jnp.float32).T.astype(jnp.bfloat16)

    cq = C // n_aux
    t_blk = t_ref[...].reshape(n_aux * I_BLOCK * cq, D)
    for p0 in range(0, n_p, P_GROUP):
        pn = min(P_GROUP, n_p - p0)
        v = jnp.dot(
            t_blk, r_ref[:, p0 * B:(p0 + pn) * B], preferred_element_type=jnp.float32
        ).astype(jnp.bfloat16)
        for dp in range(pn):
            p = p0 + dp
            for q in range(n_aux):
                for i in range(I_BLOCK):
                    r0 = (q * I_BLOCK + i) * cq
                    w_ref[p * C + q * cq:p * C + (q + 1) * cq, i * B:(i + 1) * B] = (
                        v[r0:r0 + cq, dp * B:(dp + 1) * B])
    y = jnp.dot(l_ref[...], w_ref[...], preferred_element_type=jnp.float32)
    apa = A // n_aux
    for i in range(I_BLOCK):
        for q in range(n_aux):
            out_ref[i // rpp, q, i % rpp] = y[q * apa:(q + 1) * apa, i * B:(i + 1) * B].astype(out_ref.dtype)


def local_ladder(t_all, factor_ca, factor_db, n_pair, n_aux):
    n_p = factor_ca.shape[0]
    nij = t_all.shape[1]
    rpp = nij // n_pair
    apa = A // n_aux
    t2 = t_all
    r2 = factor_db.reshape(n_p, D, B)
    l2 = factor_ca.reshape(n_p, C, A)
    steps = nij // I_BLOCK
    pb = I_BLOCK // rpp
    flops = 4 * nij * C * D * n_p * B
    kernel = functools.partial(ladder_kernel, n_p, n_aux, rpp)
    return pl.pallas_call(
        kernel,
        grid=(steps,),
        in_specs=[
            pl.BlockSpec((n_aux, I_BLOCK, C // n_aux, D), lambda g: (0, g, 0, 0)),
            pl.BlockSpec((n_p, D, B), lambda g: (0, 0, 0)),
            pl.BlockSpec((n_p, C, A), lambda g: (0, 0, 0)),
        ],
        out_specs=pl.BlockSpec((pb, n_aux, rpp, apa, B), lambda g: (g, 0, 0, 0, 0)),
        out_shape=jax.ShapeDtypeStruct((n_pair, n_aux, rpp, apa, B), jnp.bfloat16),
        scratch_shapes=[
            pltpu.VMEM((n_p * C, I_BLOCK * B), jnp.bfloat16),
            pltpu.VMEM((D, n_p * B), jnp.bfloat16),
            pltpu.VMEM((A, n_p * C), jnp.bfloat16),
        ],
        compiler_params=pltpu.CompilerParams(
            dimension_semantics=("arbitrary",), vmem_limit_bytes=48 * 1024 * 1024),
        cost_estimate=pl.CostEstimate(
            flops=flops, transcendentals=0,
            bytes_accessed=2 * (t2.size + r2.size + l2.size) + 2 * nij * A * B,
        ),
    )(t2, r2, l2)


def plan(n_pair, n_aux):
    if (n_pair, n_aux) == (64, 4):
        return [0], ([1, 2], [2, 1]), [6, 3, 5, 7, 4]
    n_bits = (n_pair * n_aux).bit_length() - 1
    rest = list(range(2, n_bits))
    return [0], ([1], [1]), rest


def xor_perm(n, b):
    return [(i, i ^ (1 << b)) for i in range(n)]


def gather_step(buf, axes, n, me, b, k):
    recv = lax.ppermute(buf, axes, xor_perm(n, b))
    low = ((me >> b) & 1) == 0
    lo = jnp.where(low, buf, recv)
    hi = jnp.where(low, recv, buf)
    return jnp.stack([lo, hi], axis=k)


def gather_bits(x, axes, n, first, pair_orders, last, target, split_axis):
    n_bits = n.bit_length() - 1
    me = lax.axis_index(axes)
    buf = x
    for k, b in enumerate(first):
        buf = gather_step(buf, axes, n, me, b, k)
    ax = len(first) + split_axis
    size = buf.shape[ax] // 2
    halves = []
    for h, tail in enumerate(pair_orders):
        part = lax.slice_in_dim(buf, h * size, (h + 1) * size, axis=ax)
        order = first + tail + last
        for k, b in enumerate(tail + last):
            part = gather_step(part, axes, n, me, b, len(first) + k)
        perm = [order.index(b) for b in target]
        halves.append(part.transpose(perm + list(range(n_bits, part.ndim))))
    return jnp.concatenate(halves, axis=n_bits + split_axis)


def reduce_step(buf, axes, n, me, live, b):
    ax = live.index(b)
    mine = (me >> b) & 1
    keep = lax.dynamic_index_in_dim(buf, mine, axis=ax, keepdims=False)
    send = lax.dynamic_index_in_dim(buf, 1 - mine, axis=ax, keepdims=False)
    wire = jnp.bfloat16 if send.size > SMALL_SEND else jnp.float32
    recv = lax.ppermute(send.astype(wire), axes, xor_perm(n, b))
    live.pop(ax)
    return keep.astype(jnp.float32) + recv.astype(jnp.float32)


def reduce_bits(y, axes, n, first, pair_orders, last):
    n_bits = n.bit_length() - 1
    me = lax.axis_index(axes)
    buf = y.reshape((2,) * n_bits + y.shape[1:])
    live = list(range(n_bits - 1, -1, -1))
    for b in first:
        buf = reduce_step(buf, axes, n, me, live, b)
    ax = len(live)
    size = buf.shape[ax] // 2
    halves = []
    for order in pair_orders:
        part = lax.slice_in_dim(buf, size * len(halves), size * (len(halves) + 1), axis=ax)
        part_live = list(live)
        for b in order:
            part = reduce_step(part, axes, n, me, part_live, b)
        halves.append(part)
    live = part_live
    buf = jnp.concatenate(halves, axis=len(live))
    for b in last:
        buf = reduce_step(buf, axes, n, me, live, b)
    return buf


def local(amplitudes, factor_ca, factor_db):
    n_pair = lax.axis_size("pair")
    n_aux = lax.axis_size("aux")
    n = n_pair * n_aux
    both = ("pair", "aux")
    first, pair_orders, last = plan(n_pair, n_aux)
    rows = amplitudes.shape[0]
    cq = C // n_aux
    q = lax.axis_index("aux")
    amps_q = lax.dynamic_slice_in_dim(amplitudes, q * cq * D, cq * D, axis=1)
    amps_q = amps_q.reshape(rows, cq, D)
    n_bits = n.bit_length() - 1
    aux_bits = n_aux.bit_length() - 1
    target = list(range(aux_bits - 1, -1, -1)) + list(range(n_bits - 1, aux_bits - 1, -1))
    t_all = gather_bits(amps_q, both, n, last[::-1], [o[::-1] for o in pair_orders], first[::-1], target, 1)
    t_all = t_all.reshape(n_aux, n_pair * rows, cq, D)
    y = local_ladder(t_all, factor_ca, factor_db, n_pair, n_aux)
    rpp = y.shape[2]
    y = y.reshape(n, rpp * y.shape[3], B)
    mine = reduce_bits(y, both, n, first, pair_orders, last).astype(jnp.bfloat16)
    return mine.reshape(rpp, -1)


def solution(mesh):
    return jax.shard_map(
        local,
        mesh=mesh,
        in_specs=(P("pair", None), P(("pair", "aux"), None), P(("pair", "aux"), None)),
        out_specs=P("pair", "aux"),
        check_vma=False,
    )
```

```python
import functools

import jax
import jax.numpy as jnp
from jax import lax
from jax.experimental import pallas as pl
from jax.experimental.pallas import tpu as pltpu
from jax.sharding import PartitionSpec as P

A = 128
B = 128
C = 128
D = 128
I_BLOCK = 16
P_GROUP = 5
SMALL_SEND = 65536


def ladder_kernel(n_p, n_aux, rpp, t_ref, fb_ref, fa_ref, out_ref, w_ref, r_ref, l_ref):
    @pl.when(pl.program_id(0) == 0)
    def _():
        for p in range(n_p):
            r_ref[:, p * B:(p + 1) * B] = fb_ref[p]
            l_ref[:, p * C:(p + 1) * C] = fa_ref[p].astype(jnp.float32).T.astype(jnp.bfloat16)

    cq = C // n_aux
    t_blk = t_ref[...].reshape(n_aux * I_BLOCK * cq, D)
    for p0 in range(0, n_p, P_GROUP):
        pn = min(P_GROUP, n_p - p0)
        v = jnp.dot(
            t_blk, r_ref[:, p0 * B:(p0 + pn) * B], preferred_element_type=jnp.float32
        ).astype(jnp.bfloat16)
        for dp in range(pn):
            p = p0 + dp
            for q in range(n_aux):
                for i in range(I_BLOCK):
                    r0 = (q * I_BLOCK + i) * cq
                    w_ref[p * C + q * cq:p * C + (q + 1) * cq, i * B:(i + 1) * B] = (
                        v[r0:r0 + cq, dp * B:(dp + 1) * B])
    y = jnp.dot(l_ref[...], w_ref[...], preferred_element_type=jnp.float32)
    apa = A // n_aux
    for i in range(I_BLOCK):
        for q in range(n_aux):
            out_ref[i // rpp, q, i % rpp] = y[q * apa:(q + 1) * apa, i * B:(i + 1) * B].astype(out_ref.dtype)


def local_ladder(t_all, factor_ca, factor_db, n_pair, n_aux):
    n_p = factor_ca.shape[0]
    nij = t_all.shape[1]
    rpp = nij // n_pair
    apa = A // n_aux
    t2 = t_all
    r2 = factor_db.reshape(n_p, D, B)
    l2 = factor_ca.reshape(n_p, C, A)
    steps = nij // I_BLOCK
    pb = I_BLOCK // rpp
    flops = 4 * nij * C * D * n_p * B
    kernel = functools.partial(ladder_kernel, n_p, n_aux, rpp)
    return pl.pallas_call(
        kernel,
        grid=(steps,),
        in_specs=[
            pl.BlockSpec((n_aux, I_BLOCK, C // n_aux, D), lambda g: (0, g, 0, 0)),
            pl.BlockSpec((n_p, D, B), lambda g: (0, 0, 0)),
            pl.BlockSpec((n_p, C, A), lambda g: (0, 0, 0)),
        ],
        out_specs=pl.BlockSpec((pb, n_aux, rpp, apa, B), lambda g: (g, 0, 0, 0, 0)),
        out_shape=jax.ShapeDtypeStruct((n_pair, n_aux, rpp, apa, B), jnp.bfloat16),
        scratch_shapes=[
            pltpu.VMEM((n_p * C, I_BLOCK * B), jnp.bfloat16),
            pltpu.VMEM((D, n_p * B), jnp.bfloat16),
            pltpu.VMEM((A, n_p * C), jnp.bfloat16),
        ],
        compiler_params=pltpu.CompilerParams(
            dimension_semantics=("arbitrary",), vmem_limit_bytes=48 * 1024 * 1024),
        cost_estimate=pl.CostEstimate(
            flops=flops, transcendentals=0,
            bytes_accessed=2 * (t2.size + r2.size + l2.size) + 2 * nij * A * B,
        ),
    )(t2, r2, l2)


def plan(n_pair, n_aux):
    if (n_pair, n_aux) == (64, 4):
        return [0], ([1, 2], [2, 1]), [6, 3, 5, 7, 4]
    n_bits = (n_pair * n_aux).bit_length() - 1
    rest = list(range(2, n_bits))
    return [0], ([1], [1]), rest


def xor_perm(n, b):
    return [(i, i ^ (1 << b)) for i in range(n)]


def gather_step(buf, axes, n, me, b, k):
    recv = lax.ppermute(buf, axes, xor_perm(n, b))
    low = ((me >> b) & 1) == 0
    lo = jnp.where(low, buf, recv)
    hi = jnp.where(low, recv, buf)
    return jnp.stack([lo, hi], axis=k)


def gather_bits(x, axes, n, first, pair_orders, last, target, split_axis):
    n_bits = n.bit_length() - 1
    me = lax.axis_index(axes)
    buf = x
    for k, b in enumerate(first):
        buf = gather_step(buf, axes, n, me, b, k)
    ax = len(first) + split_axis
    size = buf.shape[ax] // 2
    halves = []
    for h, tail in enumerate(pair_orders):
        part = lax.slice_in_dim(buf, h * size, (h + 1) * size, axis=ax)
        order = first + tail + last
        for k, b in enumerate(tail + last):
            part = gather_step(part, axes, n, me, b, len(first) + k)
        perm = [order.index(b) for b in target]
        halves.append(part.transpose(perm + list(range(n_bits, part.ndim))))
    return jnp.concatenate(halves, axis=n_bits + split_axis)


def reduce_step(buf, axes, n, me, live, b):
    ax = live.index(b)
    mine = (me >> b) & 1
    keep = lax.dynamic_index_in_dim(buf, mine, axis=ax, keepdims=False)
    send = lax.dynamic_index_in_dim(buf, 1 - mine, axis=ax, keepdims=False)
    wire = jnp.bfloat16 if send.size > SMALL_SEND else jnp.float32
    recv = lax.ppermute(send.astype(wire), axes, xor_perm(n, b))
    live.pop(ax)
    return keep.astype(jnp.float32) + recv.astype(jnp.float32)


def reduce_bits(y, axes, n, first, pair_orders, last):
    n_bits = n.bit_length() - 1
    me = lax.axis_index(axes)
    buf = y.reshape((2,) * n_bits + y.shape[1:])
    live = list(range(n_bits - 1, -1, -1))
    for b in first:
        buf = reduce_step(buf, axes, n, me, live, b)
    ax = len(live)
    size = buf.shape[ax] // 2
    halves = []
    for order in pair_orders:
        part = lax.slice_in_dim(buf, size * len(halves), size * (len(halves) + 1), axis=ax)
        part_live = list(live)
        for b in order:
            part = reduce_step(part, axes, n, me, part_live, b)
        halves.append(part)
    live = part_live
    buf = jnp.concatenate(halves, axis=len(live))
    for b in last:
        buf = reduce_step(buf, axes, n, me, live, b)
    return buf


def local(amplitudes, factor_ca, factor_db):
    n_pair = lax.axis_size("pair")
    n_aux = lax.axis_size("aux")
    n = n_pair * n_aux
    both = ("pair", "aux")
    first, pair_orders, last = plan(n_pair, n_aux)
    rows = amplitudes.shape[0]
    cq = C // n_aux
    q = lax.axis_index("aux")
    amps_q = lax.dynamic_slice_in_dim(amplitudes, q * cq * D, cq * D, axis=1)
    amps_q = amps_q.reshape(rows, cq, D)
    n_bits = n.bit_length() - 1
    aux_bits = n_aux.bit_length() - 1
    target = list(range(aux_bits - 1, -1, -1)) + list(range(n_bits - 1, aux_bits - 1, -1))
    t_all = gather_bits(amps_q, both, n, last[::-1], [o[::-1] for o in pair_orders], first[::-1], target, 1)
    t_all = t_all.reshape(n_aux, n_pair * rows, cq, D)
    y = local_ladder(t_all, factor_ca, factor_db, n_pair, n_aux)
    rpp = y.shape[2]
    y = y.reshape(n, rpp * y.shape[3], B)
    mine = reduce_bits(y, both, n, first, pair_orders, last).astype(jnp.bfloat16)
    return mine.reshape(rpp, -1)


def solution(mesh):
    return jax.shard_map(
        local,
        mesh=mesh,
        in_specs=(P("pair", None), P(("pair", "aux"), None), P(("pair", "aux"), None)),
        out_specs=P("pair", "aux"),
        check_vma=False,
    )
```

```python
import functools

import jax
import jax.numpy as jnp
from jax import lax
from jax.experimental import pallas as pl
from jax.experimental.pallas import tpu as pltpu
from jax.sharding import PartitionSpec as P

A = 128
B = 128
C = 128
D = 128
I_BLOCK = 16
P_GROUP = 5
SMALL_SEND = 0


def ladder_kernel(n_p, n_aux, rpp, t_ref, fb_ref, fa_ref, out_ref, w_ref, r_ref, l_ref):
    @pl.when(pl.program_id(0) == 0)
    def _():
        for p in range(n_p):
            r_ref[:, p * B:(p + 1) * B] = fb_ref[p]
            l_ref[:, p * C:(p + 1) * C] = fa_ref[p].astype(jnp.float32).T.astype(jnp.bfloat16)

    cq = C // n_aux
    t_blk = t_ref[...].reshape(n_aux * I_BLOCK * cq, D)
    for p0 in range(0, n_p, P_GROUP):
        pn = min(P_GROUP, n_p - p0)
        v = jnp.dot(
            t_blk, r_ref[:, p0 * B:(p0 + pn) * B], preferred_element_type=jnp.float32
        ).astype(jnp.bfloat16)
        for dp in range(pn):
            p = p0 + dp
            for q in range(n_aux):
                for i in range(I_BLOCK):
                    r0 = (q * I_BLOCK + i) * cq
                    w_ref[p * C + q * cq:p * C + (q + 1) * cq, i * B:(i + 1) * B] = (
                        v[r0:r0 + cq, dp * B:(dp + 1) * B])
    y = jnp.dot(l_ref[...], w_ref[...], preferred_element_type=jnp.float32)
    apa = A // n_aux
    for i in range(I_BLOCK):
        for q in range(n_aux):
            out_ref[i // rpp, q, i % rpp] = y[q * apa:(q + 1) * apa, i * B:(i + 1) * B].astype(out_ref.dtype)


def local_ladder(t_all, factor_ca, factor_db, n_pair, n_aux):
    n_p = factor_ca.shape[0]
    nij = t_all.shape[1]
    rpp = nij // n_pair
    apa = A // n_aux
    t2 = t_all
    r2 = factor_db.reshape(n_p, D, B)
    l2 = factor_ca.reshape(n_p, C, A)
    steps = nij // I_BLOCK
    pb = I_BLOCK // rpp
    flops = 4 * nij * C * D * n_p * B
    kernel = functools.partial(ladder_kernel, n_p, n_aux, rpp)
    return pl.pallas_call(
        kernel,
        grid=(steps,),
        in_specs=[
            pl.BlockSpec((n_aux, I_BLOCK, C // n_aux, D), lambda g: (0, g, 0, 0)),
            pl.BlockSpec((n_p, D, B), lambda g: (0, 0, 0)),
            pl.BlockSpec((n_p, C, A), lambda g: (0, 0, 0)),
        ],
        out_specs=pl.BlockSpec((pb, n_aux, rpp, apa, B), lambda g: (g, 0, 0, 0, 0)),
        out_shape=jax.ShapeDtypeStruct((n_pair, n_aux, rpp, apa, B), jnp.bfloat16),
        scratch_shapes=[
            pltpu.VMEM((n_p * C, I_BLOCK * B), jnp.bfloat16),
            pltpu.VMEM((D, n_p * B), jnp.bfloat16),
            pltpu.VMEM((A, n_p * C), jnp.bfloat16),
        ],
        compiler_params=pltpu.CompilerParams(
            dimension_semantics=("arbitrary",), vmem_limit_bytes=48 * 1024 * 1024),
        cost_estimate=pl.CostEstimate(
            flops=flops, transcendentals=0,
            bytes_accessed=2 * (t2.size + r2.size + l2.size) + 2 * nij * A * B,
        ),
    )(t2, r2, l2)


def plan(n_pair, n_aux):
    if (n_pair, n_aux) == (64, 4):
        return [0], ([1, 2], [2, 1]), [6, 3, 5, 7, 4]
    n_bits = (n_pair * n_aux).bit_length() - 1
    rest = list(range(2, n_bits))
    return [0], ([1], [1]), rest


def xor_perm(n, b):
    return [(i, i ^ (1 << b)) for i in range(n)]


def gather_step(buf, axes, n, me, b, k):
    recv = lax.ppermute(buf, axes, xor_perm(n, b))
    low = ((me >> b) & 1) == 0
    lo = jnp.where(low, buf, recv)
    hi = jnp.where(low, recv, buf)
    return jnp.stack([lo, hi], axis=k)


def gather_bits(x, axes, n, first, pair_orders, last, target, split_axis):
    n_bits = n.bit_length() - 1
    me = lax.axis_index(axes)
    buf = x
    for k, b in enumerate(first):
        buf = gather_step(buf, axes, n, me, b, k)
    ax = len(first) + split_axis
    size = buf.shape[ax] // 2
    halves = []
    for h, tail in enumerate(pair_orders):
        part = lax.slice_in_dim(buf, h * size, (h + 1) * size, axis=ax)
        order = first + tail + last
        for k, b in enumerate(tail + last):
            part = gather_step(part, axes, n, me, b, len(first) + k)
        perm = [order.index(b) for b in target]
        halves.append(part.transpose(perm + list(range(n_bits, part.ndim))))
    return jnp.concatenate(halves, axis=n_bits + split_axis)


def reduce_step(buf, axes, n, me, live, b):
    ax = live.index(b)
    mine = (me >> b) & 1
    keep = lax.dynamic_index_in_dim(buf, mine, axis=ax, keepdims=False)
    send = lax.dynamic_index_in_dim(buf, 1 - mine, axis=ax, keepdims=False)
    wire = jnp.bfloat16 if send.size > SMALL_SEND else jnp.float32
    recv = lax.ppermute(send.astype(wire), axes, xor_perm(n, b))
    live.pop(ax)
    return keep.astype(jnp.float32) + recv.astype(jnp.float32)


def reduce_bits(y, axes, n, first, pair_orders, last):
    n_bits = n.bit_length() - 1
    me = lax.axis_index(axes)
    buf = y.reshape((2,) * n_bits + y.shape[1:])
    live = list(range(n_bits - 1, -1, -1))
    for b in first:
        buf = reduce_step(buf, axes, n, me, live, b)
    ax = len(live)
    size = buf.shape[ax] // 2
    halves = []
    for order in pair_orders:
        part = lax.slice_in_dim(buf, size * len(halves), size * (len(halves) + 1), axis=ax)
        part_live = list(live)
        for b in order:
            part = reduce_step(part, axes, n, me, part_live, b)
        halves.append(part)
    live = part_live
    buf = jnp.concatenate(halves, axis=len(live))
    for b in last:
        buf = reduce_step(buf, axes, n, me, live, b)
    return buf


def local(amplitudes, factor_ca, factor_db):
    n_pair = lax.axis_size("pair")
    n_aux = lax.axis_size("aux")
    n = n_pair * n_aux
    both = ("pair", "aux")
    first, pair_orders, last = plan(n_pair, n_aux)
    rows = amplitudes.shape[0]
    cq = C // n_aux
    q = lax.axis_index("aux")
    amps_q = lax.dynamic_slice_in_dim(amplitudes, q * cq * D, cq * D, axis=1)
    amps_q = amps_q.reshape(rows, cq, D)
    n_bits = n.bit_length() - 1
    aux_bits = n_aux.bit_length() - 1
    target = list(range(aux_bits - 1, -1, -1)) + list(range(n_bits - 1, aux_bits - 1, -1))
    t_all = gather_bits(amps_q, both, n, last[::-1], [o[::-1] for o in pair_orders], first[::-1], target, 1)
    t_all = t_all.reshape(n_aux, n_pair * rows, cq, D)
    y = local_ladder(t_all, factor_ca, factor_db, n_pair, n_aux)
    rpp = y.shape[2]
    y = y.reshape(n, rpp * y.shape[3], B)
    mine = reduce_bits(y, both, n, first, pair_orders, last).astype(jnp.bfloat16)
    return mine.reshape(rpp, -1)


def solution(mesh):
    return jax.shard_map(
        local,
        mesh=mesh,
        in_specs=(P("pair", None), P(("pair", "aux"), None), P(("pair", "aux"), None)),
        out_specs=P("pair", "aux"),
        check_vma=False,
    )
```

```python
import functools

import jax
import jax.numpy as jnp
from jax import lax
from jax.experimental import pallas as pl
from jax.experimental.pallas import tpu as pltpu
from jax.sharding import PartitionSpec as P

A = 128
B = 128
C = 128
D = 128
I_BLOCK = 16
P_GROUP = 5
SMALL_SEND = 0


def ladder_kernel(n_p, n_aux, rpp, t_ref, fb_ref, fa_ref, out_ref, w_ref, r_ref, l_ref):
    @pl.when(pl.program_id(0) == 0)
    def _():
        for p in range(n_p):
            r_ref[:, p * B:(p + 1) * B] = fb_ref[p]
            l_ref[:, p * C:(p + 1) * C] = fa_ref[p].astype(jnp.float32).T.astype(jnp.bfloat16)

    cq = C // n_aux
    t_blk = t_ref[...].reshape(n_aux * I_BLOCK * cq, D)
    for p0 in range(0, n_p, P_GROUP):
        pn = min(P_GROUP, n_p - p0)
        v = jnp.dot(
            t_blk, r_ref[:, p0 * B:(p0 + pn) * B], preferred_element_type=jnp.float32
        ).astype(jnp.bfloat16)
        for dp in range(pn):
            p = p0 + dp
            for q in range(n_aux):
                for i in range(I_BLOCK):
                    r0 = (q * I_BLOCK + i) * cq
                    w_ref[p * C + q * cq:p * C + (q + 1) * cq, i * B:(i + 1) * B] = (
                        v[r0:r0 + cq, dp * B:(dp + 1) * B])
    y = jnp.dot(l_ref[...], w_ref[...], preferred_element_type=jnp.float32)
    apa = A // n_aux
    for i in range(I_BLOCK):
        for q in range(n_aux):
            out_ref[i // rpp, q, i % rpp] = y[q * apa:(q + 1) * apa, i * B:(i + 1) * B].astype(out_ref.dtype)


def local_ladder(t_all, factor_ca, factor_db, n_pair, n_aux):
    n_p = factor_ca.shape[0]
    nij = t_all.shape[1]
    rpp = nij // n_pair
    apa = A // n_aux
    t2 = t_all
    r2 = factor_db.reshape(n_p, D, B)
    l2 = factor_ca.reshape(n_p, C, A)
    steps = nij // I_BLOCK
    pb = I_BLOCK // rpp
    flops = 4 * nij * C * D * n_p * B
    kernel = functools.partial(ladder_kernel, n_p, n_aux, rpp)
    return pl.pallas_call(
        kernel,
        grid=(steps,),
        in_specs=[
            pl.BlockSpec((n_aux, I_BLOCK, C // n_aux, D), lambda g: (0, g, 0, 0)),
            pl.BlockSpec((n_p, D, B), lambda g: (0, 0, 0)),
            pl.BlockSpec((n_p, C, A), lambda g: (0, 0, 0)),
        ],
        out_specs=pl.BlockSpec((pb, n_aux, rpp, apa, B), lambda g: (g, 0, 0, 0, 0)),
        out_shape=jax.ShapeDtypeStruct((n_pair, n_aux, rpp, apa, B), jnp.bfloat16),
        scratch_shapes=[
            pltpu.VMEM((n_p * C, I_BLOCK * B), jnp.bfloat16),
            pltpu.VMEM((D, n_p * B), jnp.bfloat16),
            pltpu.VMEM((A, n_p * C), jnp.bfloat16),
        ],
        compiler_params=pltpu.CompilerParams(
            dimension_semantics=("arbitrary",), vmem_limit_bytes=48 * 1024 * 1024),
        cost_estimate=pl.CostEstimate(
            flops=flops, transcendentals=0,
            bytes_accessed=2 * (t2.size + r2.size + l2.size) + 2 * nij * A * B,
        ),
    )(t2, r2, l2)


def plan(n_pair, n_aux):
    if (n_pair, n_aux) == (64, 4):
        return [0], ([1, 2], [2, 1]), [[6, 3], [5, 7], [4]]
    n_bits = (n_pair * n_aux).bit_length() - 1
    rest = list(range(2, n_bits))
    return [0], ([1], [1]), [rest[k:k + 2] for k in range(0, len(rest), 2)]


def xor_perm(n, b):
    return [(i, i ^ (1 << b)) for i in range(n)]


def gather_step(buf, axes, n, me, b, k):
    recv = lax.ppermute(buf, axes, xor_perm(n, b))
    low = ((me >> b) & 1) == 0
    lo = jnp.where(low, buf, recv)
    hi = jnp.where(low, recv, buf)
    return jnp.stack([lo, hi], axis=k)


def gather_step4(buf, axes, n, me, b1, b2, k):
    r1 = lax.ppermute(buf, axes, xor_perm(n, b1))
    r2 = lax.ppermute(buf, axes, xor_perm(n, b2))
    r3 = lax.ppermute(buf, axes, [(i, i ^ (1 << b1) ^ (1 << b2)) for i in range(n)])
    my1 = ((me >> b1) & 1) == 1
    my2 = ((me >> b2) & 1) == 1
    rows = []
    for x1 in (False, True):
        d1 = my1 != x1
        row = []
        for x2 in (False, True):
            d2 = my2 != x2
            row.append(jnp.where(d1, jnp.where(d2, r3, r1), jnp.where(d2, r2, buf)))
        rows.append(jnp.stack(row, axis=k))
    return jnp.stack(rows, axis=k)


def gather_bits(x, axes, n, first_groups, pair_orders, last, target, split_axis):
    n_bits = n.bit_length() - 1
    me = lax.axis_index(axes)
    buf = x
    first = []
    for grp in first_groups:
        if len(grp) == 2:
            buf = gather_step4(buf, axes, n, me, grp[0], grp[1], len(first))
        else:
            buf = gather_step(buf, axes, n, me, grp[0], len(first))
        first = first + list(grp)
    ax = len(first) + split_axis
    size = buf.shape[ax] // 2
    halves = []
    for h, tail in enumerate(pair_orders):
        part = lax.slice_in_dim(buf, h * size, (h + 1) * size, axis=ax)
        order = first + tail + last
        for k, b in enumerate(tail + last):
            part = gather_step(part, axes, n, me, b, len(first) + k)
        perm = [order.index(b) for b in target]
        halves.append(part.transpose(perm + list(range(n_bits, part.ndim))))
    return jnp.concatenate(halves, axis=n_bits + split_axis)


def reduce_step(buf, axes, n, me, live, b):
    ax = live.index(b)
    mine = (me >> b) & 1
    keep = lax.dynamic_index_in_dim(buf, mine, axis=ax, keepdims=False)
    send = lax.dynamic_index_in_dim(buf, 1 - mine, axis=ax, keepdims=False)
    wire = jnp.bfloat16 if send.size > SMALL_SEND else jnp.float32
    recv = lax.ppermute(send.astype(wire), axes, xor_perm(n, b))
    live.pop(ax)
    return keep.astype(jnp.float32) + recv.astype(jnp.float32)


def reduce_step4(buf, axes, n, me, live, b1, b2):
    my1 = (me >> b1) & 1
    my2 = (me >> b2) & 1
    ax1 = live.index(b1)
    ax2 = live.index(b2) - (1 if live.index(b2) > ax1 else 0)

    def part(v1, v2):
        blk = lax.dynamic_index_in_dim(buf, v1, axis=ax1, keepdims=False)
        blk = lax.dynamic_index_in_dim(blk, v2, axis=ax2, keepdims=False)
        return blk

    total = part(my1, my2).astype(jnp.float32)
    for v1, v2, perm in (
        (1 - my1, my2, xor_perm(n, b1)),
        (my1, 1 - my2, xor_perm(n, b2)),
        (1 - my1, 1 - my2, [(i, i ^ (1 << b1) ^ (1 << b2)) for i in range(n)]),
    ):
        send = part(v1, v2)
        wire = jnp.bfloat16 if send.size > SMALL_SEND else jnp.float32
        total = total + lax.ppermute(send.astype(wire), axes, perm).astype(jnp.float32)
    live.remove(b1)
    live.remove(b2)
    return total


def reduce_bits(y, axes, n, first, pair_orders, last):
    n_bits = n.bit_length() - 1
    me = lax.axis_index(axes)
    buf = y.reshape((2,) * n_bits + y.shape[1:])
    live = list(range(n_bits - 1, -1, -1))
    for b in first:
        buf = reduce_step(buf, axes, n, me, live, b)
    ax = len(live)
    size = buf.shape[ax] // 2
    halves = []
    for order in pair_orders:
        part = lax.slice_in_dim(buf, size * len(halves), size * (len(halves) + 1), axis=ax)
        part_live = list(live)
        for b in order:
            part = reduce_step(part, axes, n, me, part_live, b)
        halves.append(part)
    live = part_live
    buf = jnp.concatenate(halves, axis=len(live))
    for grp in last:
        if len(grp) == 2:
            buf = reduce_step4(buf, axes, n, me, live, grp[0], grp[1])
        else:
            buf = reduce_step(buf, axes, n, me, live, grp[0])
    return buf


def local(amplitudes, factor_ca, factor_db):
    n_pair = lax.axis_size("pair")
    n_aux = lax.axis_size("aux")
    n = n_pair * n_aux
    both = ("pair", "aux")
    first, pair_orders, last = plan(n_pair, n_aux)
    rows = amplitudes.shape[0]
    cq = C // n_aux
    q = lax.axis_index("aux")
    amps_q = lax.dynamic_slice_in_dim(amplitudes, q * cq * D, cq * D, axis=1)
    amps_q = amps_q.reshape(rows, cq, D)
    n_bits = n.bit_length() - 1
    aux_bits = n_aux.bit_length() - 1
    target = list(range(aux_bits - 1, -1, -1)) + list(range(n_bits - 1, aux_bits - 1, -1))
    head = [grp[::-1] for grp in last[::-1]]
    t_all = gather_bits(amps_q, both, n, head, [o[::-1] for o in pair_orders], first[::-1], target, 1)
    t_all = t_all.reshape(n_aux, n_pair * rows, cq, D)
    y = local_ladder(t_all, factor_ca, factor_db, n_pair, n_aux)
    rpp = y.shape[2]
    y = y.reshape(n, rpp * y.shape[3], B)
    mine = reduce_bits(y, both, n, first, pair_orders, last).astype(jnp.bfloat16)
    return mine.reshape(rpp, -1)


def solution(mesh):
    return jax.shard_map(
        local,
        mesh=mesh,
        in_specs=(P("pair", None), P(("pair", "aux"), None), P(("pair", "aux"), None)),
        out_specs=P("pair", "aux"),
        check_vma=False,
    )
```

```python
import functools

import jax
import jax.numpy as jnp
from jax import lax
from jax.experimental import pallas as pl
from jax.experimental.pallas import tpu as pltpu
from jax.sharding import PartitionSpec as P

A = 128
B = 128
C = 128
D = 128
I_BLOCK = 16
P_GROUP = 5
SMALL_SEND = 0


def ladder_kernel(n_p, n_aux, rpp, ta_ref, tb_ref, fb_ref, fa_ref, out_ref, w_ref, r_ref, l_ref):
    @pl.when(pl.program_id(0) == 0)
    def _():
        for p in range(n_p):
            r_ref[:, p * B:(p + 1) * B] = fb_ref[p]
            l_ref[:, p * C:(p + 1) * C] = fa_ref[p].astype(jnp.float32).T.astype(jnp.bfloat16)

    cq = C // n_aux
    hq = cq // 2
    for h, t_ref in enumerate((ta_ref, tb_ref)):
        t_blk = t_ref[...].reshape(n_aux * I_BLOCK * hq, D)
        for p0 in range(0, n_p, P_GROUP):
            pn = min(P_GROUP, n_p - p0)
            v = jnp.dot(
                t_blk, r_ref[:, p0 * B:(p0 + pn) * B], preferred_element_type=jnp.float32
            ).astype(jnp.bfloat16)
            for dp in range(pn):
                p = p0 + dp
                for q in range(n_aux):
                    for i in range(I_BLOCK):
                        r0 = (q * I_BLOCK + i) * hq
                        w0 = p * C + q * cq + h * hq
                        w_ref[w0:w0 + hq, i * B:(i + 1) * B] = v[r0:r0 + hq, dp * B:(dp + 1) * B]
    y = jnp.dot(l_ref[...], w_ref[...], preferred_element_type=jnp.float32)
    apa = A // n_aux
    for i in range(I_BLOCK):
        for q in range(n_aux):
            out_ref[i // rpp, q, i % rpp] = y[q * apa:(q + 1) * apa, i * B:(i + 1) * B].astype(out_ref.dtype)


def local_ladder(t_halves, factor_ca, factor_db, n_pair, n_aux):
    n_p = factor_ca.shape[0]
    nij = t_halves[0].shape[1]
    rpp = nij // n_pair
    apa = A // n_aux
    r2 = factor_db.reshape(n_p, D, B)
    l2 = factor_ca.reshape(n_p, C, A)
    steps = nij // I_BLOCK
    pb = I_BLOCK // rpp
    flops = 4 * nij * C * D * n_p * B
    kernel = functools.partial(ladder_kernel, n_p, n_aux, rpp)
    return pl.pallas_call(
        kernel,
        grid=(steps,),
        in_specs=[
            pl.BlockSpec((n_aux, I_BLOCK, C // n_aux // 2, D), lambda g: (0, g, 0, 0)),
            pl.BlockSpec((n_aux, I_BLOCK, C // n_aux // 2, D), lambda g: (0, g, 0, 0)),
            pl.BlockSpec((n_p, D, B), lambda g: (0, 0, 0)),
            pl.BlockSpec((n_p, C, A), lambda g: (0, 0, 0)),
        ],
        out_specs=pl.BlockSpec((pb, n_aux, rpp, apa, B), lambda g: (g, 0, 0, 0, 0)),
        out_shape=jax.ShapeDtypeStruct((n_pair, n_aux, rpp, apa, B), jnp.bfloat16),
        scratch_shapes=[
            pltpu.VMEM((n_p * C, I_BLOCK * B), jnp.bfloat16),
            pltpu.VMEM((D, n_p * B), jnp.bfloat16),
            pltpu.VMEM((A, n_p * C), jnp.bfloat16),
        ],
        compiler_params=pltpu.CompilerParams(
            dimension_semantics=("arbitrary",), vmem_limit_bytes=48 * 1024 * 1024),
        cost_estimate=pl.CostEstimate(
            flops=flops, transcendentals=0,
            bytes_accessed=2 * (2 * t_halves[0].size + r2.size + l2.size) + 2 * nij * A * B,
        ),
    )(t_halves[0], t_halves[1], r2, l2)


def plan(n_pair, n_aux):
    if (n_pair, n_aux) == (64, 4):
        return [0], ([1, 2], [2, 1]), [6, 3, 5, 7, 4]
    n_bits = (n_pair * n_aux).bit_length() - 1
    rest = list(range(2, n_bits))
    return [0], ([1], [1]), rest


def xor_perm(n, b):
    return [(i, i ^ (1 << b)) for i in range(n)]


def gather_step(buf, axes, n, me, b, k):
    recv = lax.ppermute(buf, axes, xor_perm(n, b))
    low = ((me >> b) & 1) == 0
    lo = jnp.where(low, buf, recv)
    hi = jnp.where(low, recv, buf)
    return jnp.stack([lo, hi], axis=k)


def gather_bits(x, axes, n, first, pair_orders, last, target, split_axis):
    n_bits = n.bit_length() - 1
    me = lax.axis_index(axes)
    buf = x
    for k, b in enumerate(first):
        buf = gather_step(buf, axes, n, me, b, k)
    ax = len(first) + split_axis
    size = buf.shape[ax] // 2
    halves = []
    for h, tail in enumerate(pair_orders):
        part = lax.slice_in_dim(buf, h * size, (h + 1) * size, axis=ax)
        order = first + tail + last
        for k, b in enumerate(tail + last):
            part = gather_step(part, axes, n, me, b, len(first) + k)
        perm = [order.index(b) for b in target]
        halves.append(part.transpose(perm + list(range(n_bits, part.ndim))))
    return halves


def reduce_step(buf, axes, n, me, live, b):
    ax = live.index(b)
    mine = (me >> b) & 1
    keep = lax.dynamic_index_in_dim(buf, mine, axis=ax, keepdims=False)
    send = lax.dynamic_index_in_dim(buf, 1 - mine, axis=ax, keepdims=False)
    wire = jnp.bfloat16 if send.size > SMALL_SEND else jnp.float32
    recv = lax.ppermute(send.astype(wire), axes, xor_perm(n, b))
    live.pop(ax)
    return keep.astype(jnp.float32) + recv.astype(jnp.float32)


def reduce_bits(y, axes, n, first, pair_orders, last):
    n_bits = n.bit_length() - 1
    me = lax.axis_index(axes)
    buf = y.reshape((2,) * n_bits + y.shape[1:])
    live = list(range(n_bits - 1, -1, -1))
    for b in first:
        buf = reduce_step(buf, axes, n, me, live, b)
    ax = len(live)
    size = buf.shape[ax] // 2
    halves = []
    for order in pair_orders:
        part = lax.slice_in_dim(buf, size * len(halves), size * (len(halves) + 1), axis=ax)
        part_live = list(live)
        for b in order:
            part = reduce_step(part, axes, n, me, part_live, b)
        halves.append(part)
    live = part_live
    buf = jnp.concatenate(halves, axis=len(live))
    for b in last:
        buf = reduce_step(buf, axes, n, me, live, b)
    return buf


def local(amplitudes, factor_ca, factor_db):
    n_pair = lax.axis_size("pair")
    n_aux = lax.axis_size("aux")
    n = n_pair * n_aux
    both = ("pair", "aux")
    first, pair_orders, last = plan(n_pair, n_aux)
    rows = amplitudes.shape[0]
    cq = C // n_aux
    q = lax.axis_index("aux")
    amps_q = lax.dynamic_slice_in_dim(amplitudes, q * cq * D, cq * D, axis=1)
    amps_q = amps_q.reshape(rows, cq, D)
    n_bits = n.bit_length() - 1
    aux_bits = n_aux.bit_length() - 1
    target = list(range(aux_bits - 1, -1, -1)) + list(range(n_bits - 1, aux_bits - 1, -1))
    t_all = gather_bits(amps_q, both, n, last[::-1], [o[::-1] for o in pair_orders], first[::-1], target, 1)
    t_halves = [t.reshape(n_aux, n_pair * rows, cq // 2, D) for t in t_all]
    y = local_ladder(t_halves, factor_ca, factor_db, n_pair, n_aux)
    rpp = y.shape[2]
    y = y.reshape(n, rpp * y.shape[3], B)
    mine = reduce_bits(y, both, n, first, pair_orders, last).astype(jnp.bfloat16)
    return mine.reshape(rpp, -1)


def solution(mesh):
    return jax.shard_map(
        local,
        mesh=mesh,
        in_specs=(P("pair", None), P(("pair", "aux"), None), P(("pair", "aux"), None)),
        out_specs=P("pair", "aux"),
        check_vma=False,
    )
```

```python
import functools

import jax
import jax.numpy as jnp
from jax import lax
from jax.experimental import pallas as pl
from jax.experimental.pallas import tpu as pltpu
from jax.sharding import PartitionSpec as P

A = 128
B = 128
C = 128
D = 128
I_BLOCK = 16
P_GROUP = 5
SMALL_SEND = 0


def ladder_kernel(n_p, n_aux, rpp, row_of, ta_ref, tb_ref, fb_ref, fa_ref, out_ref, w_ref, r_ref, l_ref):
    @pl.when(pl.program_id(0) == 0)
    def _():
        for p in range(n_p):
            r_ref[:, p * B:(p + 1) * B] = fb_ref[p]
            l_ref[:, p * C:(p + 1) * C] = fa_ref[p].astype(jnp.float32).T.astype(jnp.bfloat16)

    cq = C // n_aux
    hq = cq // 2
    for h, t_ref in enumerate((ta_ref, tb_ref)):
        t_blk = t_ref[...].reshape(n_aux * I_BLOCK * hq, D)
        for p0 in range(0, n_p, P_GROUP):
            pn = min(P_GROUP, n_p - p0)
            v = jnp.dot(
                t_blk, r_ref[:, p0 * B:(p0 + pn) * B], preferred_element_type=jnp.float32
            ).astype(jnp.bfloat16)
            for dp in range(pn):
                p = p0 + dp
                for q in range(n_aux):
                    for i in range(I_BLOCK):
                        r0 = row_of[h][q][i] * hq
                        w0 = p * C + q * cq + h * hq
                        w_ref[w0:w0 + hq, i * B:(i + 1) * B] = v[r0:r0 + hq, dp * B:(dp + 1) * B]
    y = jnp.dot(l_ref[...], w_ref[...], preferred_element_type=jnp.float32)
    apa = A // n_aux
    for i in range(I_BLOCK):
        for q in range(n_aux):
            out_ref[i // rpp, q, i % rpp] = y[q * apa:(q + 1) * apa, i * B:(i + 1) * B].astype(out_ref.dtype)


def local_ladder(t_halves, orders, factor_ca, factor_db, n_pair, n_aux):
    n_p = factor_ca.shape[0]
    rpp = t_halves[0].shape[-3]
    nij = n_pair * rpp
    apa = A // n_aux
    aux_bits = n_aux.bit_length() - 1
    pbits = (I_BLOCK // rpp).bit_length() - 1
    in_chunk = set(range(aux_bits + pbits))

    def row_index(order, q, i):
        r = 0
        for b in order:
            if b in in_chunk:
                v = (q >> b) & 1 if b < aux_bits else ((i // rpp) >> (b - aux_bits)) & 1
                r = r * 2 + v
        return r * rpp + i % rpp

    row_of = [[[row_index(o, q, i) for i in range(I_BLOCK)] for q in range(n_aux)] for o in orders]

    def t_spec(order):
        shape = tuple(2 if b in in_chunk else 1 for b in order) + t_halves[0].shape[-3:]

        def index(g):
            bits = tuple(0 if b in in_chunk else (g >> (b - aux_bits - pbits)) & 1 for b in order)
            return bits + (0, 0, 0)
        return pl.BlockSpec(shape, index)

    r2 = factor_db.reshape(n_p, D, B)
    l2 = factor_ca.reshape(n_p, C, A)
    steps = nij // I_BLOCK
    pb = I_BLOCK // rpp
    flops = 4 * nij * C * D * n_p * B
    kernel = functools.partial(ladder_kernel, n_p, n_aux, rpp, row_of)
    return pl.pallas_call(
        kernel,
        grid=(steps,),
        in_specs=[
            t_spec(orders[0]),
            t_spec(orders[1]),
            pl.BlockSpec((n_p, D, B), lambda g: (0, 0, 0)),
            pl.BlockSpec((n_p, C, A), lambda g: (0, 0, 0)),
        ],
        out_specs=pl.BlockSpec((pb, n_aux, rpp, apa, B), lambda g: (g, 0, 0, 0, 0)),
        out_shape=jax.ShapeDtypeStruct((n_pair, n_aux, rpp, apa, B), jnp.bfloat16),
        scratch_shapes=[
            pltpu.VMEM((n_p * C, I_BLOCK * B), jnp.bfloat16),
            pltpu.VMEM((D, n_p * B), jnp.bfloat16),
            pltpu.VMEM((A, n_p * C), jnp.bfloat16),
        ],
        compiler_params=pltpu.CompilerParams(
            dimension_semantics=("arbitrary",), vmem_limit_bytes=48 * 1024 * 1024),
        cost_estimate=pl.CostEstimate(
            flops=flops, transcendentals=0,
            bytes_accessed=2 * (2 * t_halves[0].size + r2.size + l2.size) + 2 * nij * A * B,
        ),
    )(t_halves[0], t_halves[1], r2, l2)


def plan(n_pair, n_aux):
    if (n_pair, n_aux) == (64, 4):
        return [0], ([1, 2], [2, 1]), [6, 3, 5, 7, 4]
    n_bits = (n_pair * n_aux).bit_length() - 1
    rest = list(range(2, n_bits))
    return [0], ([1], [1]), rest


def xor_perm(n, b):
    return [(i, i ^ (1 << b)) for i in range(n)]


def gather_step(buf, axes, n, me, b, k):
    recv = lax.ppermute(buf, axes, xor_perm(n, b))
    low = ((me >> b) & 1) == 0
    lo = jnp.where(low, buf, recv)
    hi = jnp.where(low, recv, buf)
    return jnp.stack([lo, hi], axis=k)


def gather_bits(x, axes, n, first, pair_orders, last, target, split_axis):
    n_bits = n.bit_length() - 1
    me = lax.axis_index(axes)
    buf = x
    for k, b in enumerate(first):
        buf = gather_step(buf, axes, n, me, b, k)
    ax = len(first) + split_axis
    size = buf.shape[ax] // 2
    halves = []
    for h, tail in enumerate(pair_orders):
        part = lax.slice_in_dim(buf, h * size, (h + 1) * size, axis=ax)
        order = first + tail + last
        for k, b in enumerate(tail + last):
            part = gather_step(part, axes, n, me, b, len(first) + k)
        halves.append((part, order))
    return halves


def reduce_step(buf, axes, n, me, live, b):
    ax = live.index(b)
    mine = (me >> b) & 1
    keep = lax.dynamic_index_in_dim(buf, mine, axis=ax, keepdims=False)
    send = lax.dynamic_index_in_dim(buf, 1 - mine, axis=ax, keepdims=False)
    wire = jnp.bfloat16 if send.size > SMALL_SEND else jnp.float32
    recv = lax.ppermute(send.astype(wire), axes, xor_perm(n, b))
    live.pop(ax)
    return keep.astype(jnp.float32) + recv.astype(jnp.float32)


def reduce_bits(y, axes, n, first, pair_orders, last):
    n_bits = n.bit_length() - 1
    me = lax.axis_index(axes)
    buf = y.reshape((2,) * n_bits + y.shape[1:])
    live = list(range(n_bits - 1, -1, -1))
    for b in first:
        buf = reduce_step(buf, axes, n, me, live, b)
    ax = len(live)
    size = buf.shape[ax] // 2
    halves = []
    for order in pair_orders:
        part = lax.slice_in_dim(buf, size * len(halves), size * (len(halves) + 1), axis=ax)
        part_live = list(live)
        for b in order:
            part = reduce_step(part, axes, n, me, part_live, b)
        halves.append(part)
    live = part_live
    buf = jnp.concatenate(halves, axis=len(live))
    for b in last:
        buf = reduce_step(buf, axes, n, me, live, b)
    return buf


def local(amplitudes, factor_ca, factor_db):
    n_pair = lax.axis_size("pair")
    n_aux = lax.axis_size("aux")
    n = n_pair * n_aux
    both = ("pair", "aux")
    first, pair_orders, last = plan(n_pair, n_aux)
    rows = amplitudes.shape[0]
    cq = C // n_aux
    q = lax.axis_index("aux")
    amps_q = lax.dynamic_slice_in_dim(amplitudes, q * cq * D, cq * D, axis=1)
    amps_q = amps_q.reshape(rows, cq, D)
    n_bits = n.bit_length() - 1
    aux_bits = n_aux.bit_length() - 1
    target = list(range(aux_bits - 1, -1, -1)) + list(range(n_bits - 1, aux_bits - 1, -1))
    t_all = gather_bits(amps_q, both, n, last[::-1], [o[::-1] for o in pair_orders], first[::-1], target, 1)
    y = local_ladder([t for t, _ in t_all], [o for _, o in t_all], factor_ca, factor_db, n_pair, n_aux)
    rpp = y.shape[2]
    y = y.reshape(n, rpp * y.shape[3], B)
    mine = reduce_bits(y, both, n, first, pair_orders, last).astype(jnp.bfloat16)
    return mine.reshape(rpp, -1)


def solution(mesh):
    return jax.shard_map(
        local,
        mesh=mesh,
        in_specs=(P("pair", None), P(("pair", "aux"), None), P(("pair", "aux"), None)),
        out_specs=P("pair", "aux"),
        check_vma=False,
    )
```
